32 devices in a mesh: groups: 2 (over y), prompt: 4 (over z), enc: 4 (over x, core).
Axes of the slice: x: 2, y: 2, z: 4, core: 2. Of those that a mesh axis runs over, the one named last changes fastest.
Arguments:
- embed: bfloat16 [8192, 256], P(('groups', 'prompt', 'enc')), parts along dimension 0, may hold values from -4000 to 4000
- coords: int32 [64, 6], P(('groups', 'prompt')), parts along dimension 0, may hold values from 0 to 1023
- targets: int32 [64], P(('groups', 'prompt')), parts along dimension 0, may hold values from 0 to 7
- counts: int32 [4], replicated, may hold values from 1 to 8, 16 in all
- labels: int32 [512, 256], P('groups'), parts along dimension 0, may hold values from 0 to 7
- type_embed: float32 [4, 256], replicated, may hold values from -5 to 5
- fourier: float32 [2, 128], replicated, may hold values from -5 to 5
- wq_t: bfloat16 [256, 128], replicated, may hold values from -0.375 to 0.375
- wk_t: bfloat16 [256, 128], replicated, may hold values from -0.375 to 0.375
- wv_t: bfloat16 [256, 128], replicated, may hold values from -0.375 to 0.375
- wo_t: bfloat16 [128, 256], replicated, may hold values from -0.5 to 0.5
- wq_i: bfloat16 [256, 128], replicated, may hold values from -0.375 to 0.375
- wk_i: bfloat16 [256, 128], replicated, may hold values from -0.375 to 0.375
- wv_i: bfloat16 [256, 128], replicated, may hold values from -0.375 to 0.375
- wo_i: bfloat16 [128, 256], replicated, may hold values from -0.5 to 0.5
- gain_one: float32 [256], replicated, may hold values from 0.1 to 1.9
- gain_two: float32 [256], replicated, may hold values from 0.1 to 1.9
- gain_three: float32 [64], replicated, may hold values from 0.1 to 1.9
- up_one: bfloat16 [256, 256], replicated, may hold values from -0.375 to 0.375
- second_upsample_weight: bfloat16 [64, 128], replicated, may hold values from -0.75 to 0.75
- hyper_one: bfloat16 [256, 256], replicated, may hold values from -0.375 to 0.375
- hyper_two: bfloat16 [256, 32], replicated, may hold values from -0.375 to 0.375
Outputs:
- grad_embed: float32 [8192, 256], P(('groups', 'prompt', 'enc')), parts along dimension 0
The draws below stay inside these ranges and needn't reach their ends.
There are 2 independent parts, one for each index of `groups`. The reference program is written for one: setup_inputs(seed, part) draws one part's arguments, and reference() takes and returns one part's arrays. A program takes and returns all parts, laid end to end along the dimension named above; an argument that names none is the same for every part. Nothing has to cross between parts.
Inputs may be any that keep to these rules, and one draw needn't show every extreme that they name: Prompt index p has counts[p] live prompts, in its first slots; the counts sum to 16 and the largest is 8.
All inputs are finite; a program needn't handle non-finite values.
Results may differ from the reference program's by a relative error of at most 0.0035.
Values may be sent and summed in bfloat16 or wider, within the bound.
No kernel may reach another device: no remote copies, remote signals or barrier semaphores. Data moves between devices by JAX's collectives and lax.ppermute only.
A program may use at most 128 MiB of HBM per device.

```python
import math
import jax
import jax.numpy as jnp
import numpy as np
from jax import lax

C = 256
ATT = 128
HEADS = 8
HD = 16
UPA = 64
UPB = 32
IMG = 1024
TOKENS = 4096
MASKSIDE = 256
SLOTS = 8
PROMPTS = 16
PSLOTS = 32
NOBJ = 8
TB = 256
N_PROMPT = 4
N_ENC = 4


def draw_embed(key, part):
    base_key, scale_key, column_key = jax.random.split(key, 3)
    rows = jnp.arange(TOKENS, dtype=jnp.int32)
    enc_place = (rows // TB % N_ENC).astype(jnp.float32)
    rise = (enc_place / (N_ENC - 1)).reshape(TOKENS, 1)
    base = jnp.clip(jax.random.normal(base_key, (TOKENS, C), jnp.float32), -5.0, 5.0)
    row_scale = jnp.exp(jax.random.uniform(scale_key, (TOKENS, 1), jnp.float32, -0.4, 0.4))
    row_scale = row_scale * jnp.exp(rise * math.log(3.0))
    column_scale = jnp.exp(jax.random.uniform(column_key, (1, C), jnp.float32, -0.3, 0.3))
    values = base * row_scale * column_scale
    return values.astype(jnp.bfloat16)


def plant(entries, key, low, high):
    longest = entries.shape.index(max(entries.shape))
    spots = []
    for shift in (0, 1):
        where = [jax.random.randint(jax.random.fold_in(key, axis), (), 0, length) for axis, length in enumerate(entries.shape)]
        where[longest] = (where[longest] + shift) % entries.shape[longest]
        spots.append(tuple(where))
    return entries.at[spots[0]].set(low).at[spots[1]].set(high)


def profile(count, total, bound, skew):
    loads = [(1 << 20) // math.isqrt(rank ** skew) + 1 for rank in range(2, count + 1)]
    spare, given = total - bound - (count - 1), [1] * (count - 1)
    while spare > 0:
        free = [i for i in range(count - 1) if given[i] < bound]
        mass, left = sum([loads[i] for i in free]), spare
        for i in free:
            more = min(bound - given[i], max(1, left * loads[i] // mass), spare)
            given[i] = given[i] + more
            spare = spare - more
    return np.array([bound] + given)


def ragged(key, amount, total, most, skew):
    if amount == 2:
        one = jax.random.randint(key, (), max(1, total - most), min(most, total - 1) + 1)
        return jnp.stack([one, total - one])
    lengths = jnp.asarray(profile(amount, total, most, skew), jnp.int32)
    couples = (amount - 1) // 2
    donor, taker = lengths[1:1 + 2 * couples:2], lengths[2:2 + 2 * couples:2]
    margin = jnp.minimum(donor - 1, most - taker)
    moved = jax.random.randint(jax.random.fold_in(key, 1), (couples,), 0, 1 << 20) % (margin + 1)
    lengths = lengths.at[1:1 + 2 * couples:2].set(donor - moved).at[2:2 + 2 * couples:2].set(taker + moved)
    return lengths[jax.random.permutation(jax.random.fold_in(key, 2), amount)]


def bell_draw(key, extent, scale, limit, kind=jnp.bfloat16):
    return jnp.clip(scale * jax.random.normal(key, extent, jnp.float32), -limit, limit).astype(kind)


def setup_inputs(seed: int = 0, part: int = 0) -> dict:
    splits = jax.random.split(jax.random.key(seed), 23)
    part_keys = jax.random.split(jax.random.fold_in(splits[22], part), 23)
    embed = draw_embed(jax.random.fold_in(jax.random.fold_in(splits[22], part), 71), part)
    coords = plant(jax.random.randint(part_keys[1], (PSLOTS, 6), 0, IMG), jax.random.fold_in(part_keys[1], 1), 0, IMG - 1).astype(jnp.int32)
    targets = plant(jax.random.randint(part_keys[2], (PSLOTS,), 0, NOBJ), jax.random.fold_in(part_keys[2], 1), 0, NOBJ - 1).astype(jnp.int32)
    counts = ragged(splits[3], N_PROMPT, PROMPTS, SLOTS, 2).astype(jnp.int32)
    labels = plant(jax.random.randint(part_keys[4], (MASKSIDE, MASKSIDE), 0, NOBJ), jax.random.fold_in(part_keys[4], 1), 0, NOBJ - 1).astype(jnp.int32)
    type_embed = bell_draw(splits[5], (4, C), 1.0, 5.0, jnp.float32)
    fourier = bell_draw(splits[6], (2, C // 2), 1.0, 5.0, jnp.float32)
    wq_t = bell_draw(splits[7], (C, ATT), C ** -0.5, 0.375)
    wk_t = bell_draw(splits[8], (C, ATT), C ** -0.5, 0.375)
    wv_t = bell_draw(splits[9], (C, ATT), C ** -0.5, 0.375)
    wo_t = bell_draw(splits[10], (ATT, C), ATT ** -0.5, 0.5)
    wq_i = bell_draw(splits[11], (C, ATT), C ** -0.5, 0.375)
    wk_i = bell_draw(splits[12], (C, ATT), C ** -0.5, 0.375)
    wv_i = bell_draw(splits[13], (C, ATT), C ** -0.5, 0.375)
    wo_i = bell_draw(splits[14], (ATT, C), ATT ** -0.5, 0.5)
    gain_one = jnp.clip(1.0 + 0.18 * jax.random.normal(splits[15], (C,), jnp.float32), 0.1, 1.9)
    gain_two = jnp.clip(1.0 + 0.18 * jax.random.normal(splits[16], (C,), jnp.float32), 0.1, 1.9)
    gain_three = jnp.clip(1.0 + 0.18 * jax.random.normal(splits[17], (UPA,), jnp.float32), 0.1, 1.9)
    up_one = bell_draw(splits[18], (C, 4 * UPA), C ** -0.5, 0.375)
    second_upsample_weight = bell_draw(splits[19], (UPA, 4 * UPB), UPA ** -0.5, 0.75)
    hyper_one = bell_draw(splits[20], (C, C), C ** -0.5, 0.375)
    hyper_two = bell_draw(splits[21], (C, UPB), C ** -0.5, 0.375)
    return {"embed": embed, "coords": coords, "targets": targets, "counts": counts, "labels": labels, "type_embed": type_embed, "fourier": fourier, "wq_t": wq_t, "wk_t": wk_t, "wv_t": wv_t, "wo_t": wo_t, "wq_i": wq_i, "wk_i": wk_i, "wv_i": wv_i, "wo_i": wo_i, "gain_one": gain_one, "gain_two": gain_two, "gain_three": gain_three, "up_one": up_one, "second_upsample_weight": second_upsample_weight, "hyper_one": hyper_one, "hyper_two": hyper_two}


highest_value = lax.Precision.HIGHEST
epsilon = 1e-05

def layer_norm(values, gain):
    centered = values - lax.optimization_barrier(jnp.mean(values, axis=-1, keepdims=True))
    variance = lax.optimization_barrier(jnp.mean(centered * centered, axis=-1, keepdims=True))
    return centered * lax.rsqrt(variance + epsilon) * gain

def fourier_code(pixel_pair, fourier):
    scaled = 2.0 * ((pixel_pair.astype(jnp.float32) + 0.5) / IMG) - 1.0
    angles = 2.0 * math.pi * jnp.dot(scaled, fourier, precision=highest_value)
    return jnp.concatenate([jnp.sin(angles), jnp.cos(angles)], axis=-1)

def prompt_tokens(corner_rows, type_embed, fourier):
    point_code = fourier_code(corner_rows[..., 0:2], fourier) + type_embed[1]
    first_code = fourier_code(corner_rows[..., 2:4], fourier) + type_embed[2]
    second_code = fourier_code(corner_rows[..., 4:6], fourier) + type_embed[3]
    output_token = jnp.broadcast_to(type_embed[0], point_code.shape)
    return jnp.stack([output_token, point_code, first_code, second_code], axis=-2)

def token_pixel_scores(labels):
    side = labels.shape[0] // 4
    grid_view = labels.reshape(side, 2, 2, side, 2, 2)
    grid_view = jnp.transpose(grid_view, (0, 3, 1, 4, 2, 5))
    return grid_view.reshape(side * side, 4, 4)

def token_side(tokens_zero, key_image, value_image, wq_t, wo_t, gain_one):
    head_scale = HD ** (-0.5)
    queries = jnp.dot(tokens_zero, wq_t.astype(jnp.float32), precision=highest_value).reshape(-1, HEADS, HD)
    scores = jnp.einsum('rhd,jhd->rhj', queries, key_image.reshape(-1, HEADS, HD), precision=highest_value) * head_scale
    attention = jax.nn.softmax(scores, axis=-1)
    gathered = jnp.einsum('rhj,jhd->rhd', attention, value_image.reshape(-1, HEADS, HD), precision=highest_value)
    update = jnp.dot(gathered.reshape(tokens_zero.shape[0], -1), wo_t.astype(jnp.float32), precision=highest_value)
    return layer_norm(tokens_zero + update, gain_one)

def image_side(query_image, image_float, tokens_one, truth, live_flag, side_weights):
    wk_i, wv_i, wo_i, gain_two, up_one, gain_three, second_upsample_weight, hyper_one, hyper_two = side_weights
    head_scale = HD ** (-0.5)
    row_count = query_image.shape[0]
    token_keys = jnp.dot(tokens_one, wk_i.astype(jnp.float32), precision=highest_value).reshape(-1, HEADS, HD)
    token_values = jnp.dot(tokens_one, wv_i.astype(jnp.float32), precision=highest_value).reshape(-1, HEADS, HD)
    scores = jnp.einsum('jhd,rhd->jhr', query_image.reshape(row_count, HEADS, HD), token_keys, precision=highest_value) * head_scale
    attention = jax.nn.softmax(scores, axis=-1)
    mixed = jnp.einsum('jhr,rhd->jhd', attention, token_values, precision=highest_value).reshape(row_count, -1).astype(jnp.bfloat16)
    update = jnp.dot(mixed, wo_i, preferred_element_type=jnp.float32)
    image_one = layer_norm(image_float + update, gain_two).astype(jnp.bfloat16)
    lifted = jnp.dot(image_one, up_one, preferred_element_type=jnp.float32).reshape(row_count, 4, -1)
    first_activation = jax.nn.gelu(layer_norm(lifted, gain_three), approximate=False).astype(jnp.bfloat16)
    second_result = jnp.einsum('oij,jp->oip', first_activation.astype(jnp.float32), second_upsample_weight.astype(jnp.float32), precision=highest_value)
    features = jax.nn.gelu(second_result, approximate=False).reshape(row_count, 4, 4, -1)
    hidden = jax.nn.relu(jnp.dot(tokens_one[0], hyper_one.astype(jnp.float32), precision=highest_value))
    hyper = jnp.dot(hidden, hyper_two.astype(jnp.float32), precision=highest_value)
    logits = jnp.einsum('tasc,c->tas', features, hyper, precision=highest_value)
    losses = jax.nn.softplus(logits) - truth * logits
    return jnp.sum(losses) * live_flag * 0.25

def reference(embed, coords, targets, counts, labels, type_embed, fourier, wq_t, wk_t, wv_t, wo_t, wq_i, wk_i, wv_i, wo_i, gain_one, gain_two, gain_three, up_one, second_upsample_weight, hyper_one, hyper_two):
    key_image = jnp.dot(embed, wk_t, preferred_element_type=jnp.float32)
    value_image = jnp.dot(embed, wv_t, preferred_element_type=jnp.float32)
    query_image = jnp.dot(embed, wq_i, preferred_element_type=jnp.float32)
    image_float = embed.astype(jnp.float32)
    pixels = token_pixel_scores(labels)
    ends = jnp.cumsum(counts).astype(jnp.int32)
    numbers = jnp.arange(PROMPTS, dtype=jnp.int32)
    owners = lax.optimization_barrier(jnp.sum((ends[None, :] <= numbers[:, None]).astype(jnp.int32), axis=1)).astype(jnp.int32)
    starts = jnp.take(ends, owners) - jnp.take(counts, owners)
    slot_index = (owners * SLOTS + numbers - starts).astype(jnp.int32)
    chosen_rows = jnp.take(coords, slot_index, axis=0)
    chosen_targets = jnp.take(targets, slot_index)
    side_weights = (wk_i, wv_i, wo_i, gain_two, up_one, gain_three, second_upsample_weight, hyper_one, hyper_two)

    def single_prompt(carry, inputs):
        corner_row, target = inputs
        tokens_zero = prompt_tokens(corner_row, type_embed, fourier)
        truth = (pixels == target).astype(jnp.float32)

        def loss_of(query_arg, key_arg, value_arg, image_arg):
            tokens_one = token_side(tokens_zero, key_arg, value_arg, wq_t, wo_t, gain_one)
            return image_side(query_arg, image_arg, tokens_one, truth, 1.0, side_weights)
        _, pullback = jax.vjp(loss_of, query_image, key_image, value_image, image_float)
        grads = pullback(jnp.ones((), jnp.float32))
        return (tuple((total + piece_grad for total, piece_grad in zip(carry, grads))), None)
    initial = (jnp.zeros_like(query_image), jnp.zeros_like(key_image), jnp.zeros_like(value_image), jnp.zeros_like(image_float))
    sums, _ = lax.scan(single_prompt, initial, (chosen_rows, chosen_targets))
    d_query, d_key, d_value, d_image = sums
    grad_embed = d_image + jnp.dot(d_query, wq_i.astype(jnp.float32).T, precision=highest_value)
    grad_embed = grad_embed + jnp.dot(d_key, wk_t.astype(jnp.float32).T, precision=highest_value)
    grad_embed = grad_embed + jnp.dot(d_value, wv_t.astype(jnp.float32).T, precision=highest_value)
    return grad_embed
```

```python
import math

import jax
import jax.numpy as jnp
from jax import lax
from jax.sharding import PartitionSpec as P

HEADS = 8
HD = 16
IMG = 1024


highest_value = lax.Precision.HIGHEST
epsilon = 1e-05


def joined(array, axis, combine):
    everything = jax.tree.map(lambda part: lax.all_gather(part, axis), array)
    leading = jax.tree.map(lambda part: part[0], everything)

    def step(k, so_far):
        return combine(so_far, jax.tree.map(lambda part: part[k], everything))

    return lax.fori_loop(1, lax.axis_size(axis), step, leading)


def layer_norm(values, gain):
    centered = values - jnp.mean(values, axis=-1, keepdims=True)
    variance = jnp.mean(centered * centered, axis=-1, keepdims=True)
    return centered * lax.rsqrt(variance + epsilon) * gain


def fourier_code(pixel_pair, fourier):
    scaled = 2.0 * ((pixel_pair.astype(jnp.float32) + 0.5) / IMG) - 1.0
    angles = 2.0 * math.pi * jnp.dot(scaled, fourier, precision=highest_value)
    return jnp.concatenate([jnp.sin(angles), jnp.cos(angles)], axis=-1)


def prompt_tokens(corner_rows, type_embed, fourier):
    point_code = fourier_code(corner_rows[..., 0:2], fourier) + type_embed[1]
    first_code = fourier_code(corner_rows[..., 2:4], fourier) + type_embed[2]
    second_code = fourier_code(corner_rows[..., 4:6], fourier) + type_embed[3]
    output_token = jnp.broadcast_to(type_embed[0], point_code.shape)
    return jnp.stack([output_token, point_code, first_code, second_code], axis=-2)


def token_pixel_scores(labels):
    side = labels.shape[0] // 4
    grid_view = labels.reshape(side, 2, 2, side, 2, 2)
    grid_view = jnp.transpose(grid_view, (0, 3, 1, 4, 2, 5))
    return grid_view.reshape(side * side, 4, 4)


def combine_parts(first, second_result):
    top_first, first_running_total, accum_first = first
    top_second, total_second, accum_second = second_result
    top_both = jnp.maximum(top_first, top_second)
    factor_first = jnp.exp(top_first - top_both)
    factor_second = jnp.exp(top_second - top_both)
    total_both = first_running_total * factor_first + total_second * factor_second
    accum_both = accum_first * factor_first[..., None] + accum_second * factor_second[..., None]
    return (top_both, total_both, accum_both)


def image_side(query_image, image_float, tokens_one, truth, live_flag, side_weights):
    wk_i, wv_i, wo_i, gain_two, up_one, gain_three, second_upsample_weight, hyper_one, hyper_two = (
        side_weights
    )
    head_scale = HD ** (-0.5)
    row_count = query_image.shape[0]
    token_keys = jnp.dot(tokens_one, wk_i.astype(jnp.float32), precision=highest_value).reshape(
        -1, HEADS, HD
    )
    token_values = jnp.dot(tokens_one, wv_i.astype(jnp.float32), precision=highest_value).reshape(
        -1, HEADS, HD
    )
    scores = (
        jnp.einsum(
            "jhd,rhd->jhr",
            query_image.reshape(row_count, HEADS, HD),
            token_keys,
            precision=highest_value,
        )
        * head_scale
    )
    attention = jax.nn.softmax(scores, axis=-1)
    mixed = (
        jnp.einsum("jhr,rhd->jhd", attention, token_values, precision=highest_value)
        .reshape(row_count, -1)
        .astype(jnp.bfloat16)
    )
    update = jnp.dot(mixed, wo_i, preferred_element_type=jnp.float32)
    image_one = layer_norm(image_float + update, gain_two).astype(jnp.bfloat16)
    lifted = jnp.dot(image_one, up_one, preferred_element_type=jnp.float32).reshape(
        row_count, 4, -1
    )
    first_activation = jax.nn.gelu(layer_norm(lifted, gain_three), approximate=False).astype(
        jnp.bfloat16
    )
    second_result = jnp.einsum(
        "oij,jp->oip", first_activation, second_upsample_weight, preferred_element_type=jnp.float32
    )
    features = jax.nn.gelu(second_result, approximate=False).reshape(row_count, 4, 4, -1)
    hidden = jax.nn.relu(
        jnp.dot(tokens_one[0], hyper_one.astype(jnp.float32), precision=highest_value)
    )
    hyper = jnp.dot(hidden, hyper_two.astype(jnp.float32), precision=highest_value)
    logits = jnp.einsum("tasc,c->tas", features, hyper, precision=highest_value)
    losses = jax.nn.softplus(logits) - truth * logits
    return jnp.sum(losses) * live_flag * 0.25


def on_device(
    embed,
    coords,
    targets,
    counts,
    labels,
    type_embed,
    fourier,
    wq_t,
    wk_t,
    wv_t,
    wo_t,
    wq_i,
    wk_i,
    wv_i,
    wo_i,
    gain_one,
    gain_two,
    gain_three,
    up_one,
    second_upsample_weight,
    hyper_one,
    hyper_two,
):
    both = ("prompt", "enc")
    prompt_count = lax.axis_size("prompt")
    enc_count = lax.axis_size("enc")
    prompt_place = lax.axis_index("prompt")
    enc_place = lax.axis_index("enc")
    block_rows = embed.shape[0]
    slot_count = coords.shape[0]
    head_scale = HD ** (-0.5)
    live_total = prompt_count * slot_count // 2
    chunk = math.gcd(live_total, max(1, 1024 // block_rows))
    image_float = embed.astype(jnp.float32)
    key_image = jnp.dot(embed, wk_t, preferred_element_type=jnp.float32)
    value_image = jnp.dot(embed, wv_t, preferred_element_type=jnp.float32)
    query_image = jnp.dot(embed, wq_i, preferred_element_type=jnp.float32)
    local_rows = block_rows
    pixel_all = token_pixel_scores(labels)
    own_pixels = lax.dynamic_slice_in_dim(
        pixel_all, (prompt_place * enc_count + enc_place) * block_rows, block_rows, 0
    )
    all_coords = lax.all_gather(coords, "prompt", axis=0, tiled=True)
    all_targets = lax.all_gather(targets, "prompt", axis=0, tiled=True)
    ends = jnp.cumsum(counts).astype(jnp.int32)
    numbers = jnp.arange(live_total, dtype=jnp.int32)
    owners = jnp.sum((ends[None, :] <= numbers[:, None]).astype(jnp.int32), axis=1)
    starts = jnp.take(ends, owners) - jnp.take(counts, owners)
    slot_index = (owners * slot_count + numbers - starts).astype(jnp.int32)
    chosen_rows = jnp.take(all_coords, slot_index, axis=0)
    chosen_targets = jnp.take(all_targets, slot_index)
    tokens_zero = prompt_tokens(chosen_rows, type_embed, fourier)
    prompt_number = tokens_zero.shape[0]
    flat_tokens = tokens_zero.reshape(prompt_number * 4, -1)
    queries = jnp.dot(flat_tokens, wq_t.astype(jnp.float32), precision=highest_value).reshape(
        -1, HEADS, HD
    )
    key_heads = key_image.reshape(local_rows, HEADS, HD)
    value_heads = value_image.reshape(local_rows, HEADS, HD)
    scores = jnp.einsum("rhd,jhd->rhj", queries, key_heads, precision=highest_value) * head_scale
    local_top = jnp.max(scores, axis=-1)
    global_top = lax.pmax(local_top, both)
    shifted = jnp.exp(scores - global_top[..., None])
    local_total = jnp.sum(shifted, axis=-1)
    local_accum = jnp.einsum("rhj,jhd->rhd", shifted, value_heads, precision=highest_value)
    global_total, global_accum = lax.psum((local_total, local_accum), both)
    gathered = global_accum / global_total[..., None]
    wo_t_float = wo_t.astype(jnp.float32)
    update = jnp.dot(gathered.reshape(prompt_number * 4, -1), wo_t_float, precision=highest_value)

    def token_norm(values):
        return layer_norm(values, gain_one)

    tokens_one, norm_pull = jax.vjp(token_norm, flat_tokens + update)
    side_weights = (
        wk_i,
        wv_i,
        wo_i,
        gain_two,
        up_one,
        gain_three,
        second_upsample_weight,
        hyper_one,
        hyper_two,
    )

    def prompt_loss(query_arg, image_arg, tokens_row, target):
        truth = (own_pixels == target).astype(jnp.float32)
        return image_side(query_arg, image_arg, tokens_row, truth, 1.0, side_weights)

    def chunk_step(carry, inputs):
        tokens_rows, chunk_targets = inputs

        def loss_of(query_arg, image_arg, tokens_arg):
            losses = jax.vmap(prompt_loss, in_axes=(None, None, 0, 0))(
                query_arg, image_arg, tokens_arg, chunk_targets
            )
            return jnp.sum(losses)

        _, pullback = jax.vjp(loss_of, query_image, image_float, tokens_rows)
        d_query, d_image, d_tokens = pullback(jnp.ones((), jnp.float32))
        return ((carry[0] + d_query, carry[1] + d_image), d_tokens)

    initial = (jnp.zeros_like(query_image), jnp.zeros_like(image_float))
    sums, token_parts = lax.scan(
        chunk_step,
        initial,
        (
            tokens_one.reshape(prompt_number // chunk, chunk, 4, -1),
            chosen_targets.reshape(prompt_number // chunk, chunk),
        ),
    )
    query_grad, image_grad = sums
    token_grad = lax.psum(token_parts, both)
    (d_residual,) = norm_pull(token_grad.reshape(prompt_number * 4, -1))
    d_gathered = jnp.dot(d_residual, wo_t_float.T, precision=highest_value).reshape(-1, HEADS, HD)
    probs = shifted / global_total[..., None]
    d_probs = jnp.einsum("rhd,jhd->rhj", d_gathered, value_heads, precision=highest_value)
    delta_term = jnp.sum(d_gathered * gathered, axis=-1)
    d_scores = probs * (d_probs - delta_term[..., None]) * head_scale
    key_grad = jnp.einsum("rhj,rhd->jhd", d_scores, queries, precision=highest_value).reshape(
        local_rows, -1
    )
    value_grad = jnp.einsum("rhj,rhd->jhd", probs, d_gathered, precision=highest_value).reshape(
        local_rows, -1
    )
    wq_i_float = wq_i.astype(jnp.float32)
    wk_t_float = wk_t.astype(jnp.float32)
    wv_t_float = wv_t.astype(jnp.float32)
    result = image_grad
    result = result + jnp.dot(query_grad, wq_i_float.T, precision=highest_value)
    result = result + jnp.dot(key_grad, wk_t_float.T, precision=highest_value)
    result = result + jnp.dot(value_grad, wv_t_float.T, precision=highest_value)
    return result


def solution(mesh):
    in_specs = (
        P(("groups", "prompt", "enc"), None),
        P(("groups", "prompt"), None),
        P(("groups", "prompt")),
        P(),
        P("groups", None),
        P(),
        P(),
        P(),
        P(),
        P(),
        P(),
        P(),
        P(),
        P(),
        P(),
        P(),
        P(),
        P(),
        P(),
        P(),
        P(),
        P(),
    )
    out_specs = P(("groups", "prompt", "enc"), None)
    return jax.shard_map(
        on_device, mesh=mesh, in_specs=in_specs, out_specs=out_specs, check_vma=False
    )
```
